256 devices in a mesh: seq: 64 (over z_hi, x, y, core), tp: 4 (over z_lo).
Axes of the slice: x: 4, y: 4, z: 8 (z_hi: 2, z_lo: 4; z = z_hi * 4 + z_lo), core: 2. Of those that a mesh axis runs over, the one named last changes fastest.
Arguments:
- query_rows: bfloat16 [16384, 4096], P('seq', 'tp'), may hold values from -6 to 6
- key_rows: bfloat16 [16384, 4096], P('seq', 'tp'), may hold values from -6 to 6
- value_rows: bfloat16 [16384, 4096], P('seq', 'tp'), may hold values from -6 to 6
- short_filter: float32 [3, 3, 4096], P(None, None, 'tp'), may hold values from -3 to 3
- long_filter: bfloat16 [16384, 4096], P('seq', 'tp'), may hold values from -1.1 to 1.1, as said below
- skip_gain: float32 [4096], P('tp'), may hold values from -4 to 4
- out_weight: bfloat16 [4096, 4096], P('seq', 'tp'), may hold values from -0.09375 to 0.09375
Outputs:
- projected: bfloat16 [16384, 4096], P('seq', 'tp')
The draws below stay inside these ranges and needn't reach their ends.
Inputs may be any that keep to these rules, and one draw needn't show every extreme that they name: `long_filter`: taps of the long filter.
All inputs are finite; a program needn't handle non-finite values.
Results may differ from the reference program's by a relative error of at most 0.0061.
Values may be sent and summed in bfloat16 or wider, within the bound.
No kernel may reach another device: no remote copies, remote signals or barrier semaphores. Data moves between devices by JAX's collectives and lax.ppermute only.
A program may use at most 64 MiB of HBM per device.

```python
import math
import jax
import jax.numpy as jnp
from jax import lax

D = 4096
LEN = 16384


def draw_long_filter(key, part):
    key_rate = jax.random.fold_in(key, 11)
    key_taps = jax.random.fold_in(key, 23)
    log_rate = jax.random.uniform(key_rate, (D,), jnp.float32, math.log(0.5 / LEN), math.log(1.0 / 30.0))
    taps = jax.random.truncated_normal(key_taps, -4.0, 4.0, (LEN, D), jnp.float32)
    rate = jnp.exp(log_rate)
    position = jnp.arange(LEN, dtype=jnp.float32)[:, None]
    envelope = jnp.sqrt(2.0 * rate)[None, :] * jnp.exp(-rate[None, :] * position)
    return (taps * envelope).astype(jnp.bfloat16)


def levels(key, extent, pieces, least, high):
    def one(dim, blocks):
        heights = jax.random.uniform(jax.random.fold_in(jax.random.fold_in(key, 6), dim), (blocks,), jnp.float32, least / len(pieces), high / len(pieces))
        return jnp.repeat(jnp.exp(heights), extent[dim] // blocks).reshape((-1,) + (1,) * (len(extent) - dim - 1))

    gain = one(*pieces[0])
    for cut in pieces[1:]:
        gain = gain * one(*cut)
    return gain


def centred(key, shape, spread, most, cuts=(), kind=jnp.bfloat16):
    values = spread * jax.random.normal(key, shape, jnp.float32)
    if cuts:
        values = values * levels(key, shape, cuts, -0.22, 0.18)
    return jnp.clip(values, -most, most).astype(kind)


def setup_inputs(seed: int = 0) -> dict:
    keys = jax.random.split(jax.random.key(seed), 8)
    query_rows = centred(keys[0], (LEN, D), 1.0, 6.0, ((0, 64), (1, 4)))
    key_rows = centred(keys[1], (LEN, D), 1.0, 6.0, ((0, 64), (1, 4)))
    value_rows = centred(keys[2], (LEN, D), 1.0, 6.0, ((0, 64), (1, 4)))
    short_filter = centred(keys[3], (3, 3, D), 0.6, 3.0, ((2, 4),), jnp.float32)
    long_filter = draw_long_filter(jax.random.fold_in(keys[7], 71), 0)
    skip_gain = centred(keys[5], (D,), 1.0, 4.0, ((0, 4),), jnp.float32)
    out_weight = centred(keys[6], (D, D), D ** -0.5, 0.09375, ((0, 64), (1, 4)))
    return {"query_rows": query_rows, "key_rows": key_rows, "value_rows": value_rows, "short_filter": short_filter, "long_filter": long_filter, "skip_gain": skip_gain, "out_weight": out_weight}


def causal_short(rows, taps):
    values = rows.astype(jnp.float32)
    padding = jnp.zeros((2, rows.shape[1]), jnp.float32)
    extended = jnp.concatenate([padding, values], 0)
    return taps[0] * extended[2:] + taps[1] * extended[1:-1] + taps[2] * extended[:-2]


def long_conv(gated, long_filter):
    length, channels = gated.shape
    period = 2 * length
    blocks = channels // 64
    signal = gated.reshape(length, blocks, 64).transpose(1, 0, 2)
    taps = long_filter.reshape(length, blocks, 64).transpose(1, 0, 2)

    def one_block(pair):
        signal_block, taps_block = pair
        signal_freq = jnp.fft.rfft(signal_block.astype(jnp.float32), n=period, axis=0)
        taps_freq = jnp.fft.rfft(taps_block.astype(jnp.float32), n=period, axis=0)
        result = jnp.fft.irfft(signal_freq * taps_freq, n=period, axis=0)[:length]
        return result.astype(jnp.bfloat16)

    result = lax.map(one_block, (signal, taps))
    return result.transpose(1, 0, 2).reshape(length, channels)


def reference(query_rows, key_rows, value_rows, short_filter, long_filter, skip_gain, out_weight):
    query_mix = causal_short(query_rows, short_filter[:, 0, :])
    key_mix = causal_short(key_rows, short_filter[:, 1, :])
    value_mix = causal_short(value_rows, short_filter[:, 2, :])
    gated = (key_mix * value_mix).astype(jnp.bfloat16)
    conv = long_conv(gated, long_filter)
    inner = (query_mix * (conv.astype(jnp.float32) + skip_gain * gated.astype(jnp.float32))).astype(jnp.bfloat16)
    return jnp.dot(inner, out_weight, preferred_element_type=jnp.float32).astype(jnp.bfloat16)
```

```python
import math

import numpy as np
import jax
import jax.numpy as jnp
from jax import lax
from jax.sharding import PartitionSpec as P

TRANSFORM_PRECISION = lax.Precision.HIGH


def shifted(value, axis, by):
    size = lax.axis_size(axis)
    pairs = [(i, i + by) for i in range(size) if 0 <= i + by < size]
    return lax.ppermute(value, axis, pairs)


def make_tables(blocks, tokens):
    outer = 2 * blocks
    period = outer * tokens
    k1 = np.arange(outer, dtype=np.int64)
    n1 = np.arange(blocks, dtype=np.int64)
    n2 = np.arange(tokens, dtype=np.int64)
    first = 2.0 * np.pi * ((k1[:, None] * n1[None, :]) % outer) / outer
    first_table = np.concatenate([np.cos(first), -np.sin(first)], 0)
    twist = 2.0 * np.pi * ((k1[:, None] * n2[None, :]) % period) / period
    twist_cos = np.cos(twist)[:, None, :]
    twist_sin = np.sin(twist)[:, None, :]
    inner = 2.0 * np.pi * ((n2[:, None] * n2[None, :]) % tokens) / tokens
    b_cos = np.cos(inner)
    b_sin = np.sin(inner)
    forward = np.block([[b_cos, -b_sin], [b_sin, b_cos]])
    backward = np.block([[b_cos, b_sin], [-b_sin, b_cos]])
    last = 2.0 * np.pi * ((n1[:, None] * k1[None, :]) % outer) / outer
    last_table = np.concatenate([np.cos(last), -np.sin(last)], 1) / period
    as32 = lambda a: jnp.asarray(a, jnp.float32)
    return tuple(as32(a) for a in (first_table, twist_cos, twist_sin, forward, backward, last_table))


def dot(a, b):
    return jnp.dot(a, b, precision=TRANSFORM_PRECISION, preferred_element_type=jnp.float32)


def long_conv(pieces, per_device, tables):
    first_table, twist_cos, twist_sin, forward, backward, last_table = tables
    blocks, both, tokens = pieces.shape
    outer = 2 * blocks
    spec = dot(first_table, pieces.reshape(blocks, both * tokens)).reshape(2, outer, both, tokens)
    s_real, s_imag = spec[0], spec[1]
    w_real = s_real * twist_cos + s_imag * twist_sin
    w_imag = s_imag * twist_cos - s_real * twist_sin
    twisted = jnp.concatenate([w_real, w_imag], -1).reshape(outer * both, 2 * tokens)
    u = dot(twisted, forward).reshape(outer, both, 2 * tokens)
    u_real, u_imag = u[:, :per_device, :tokens], u[:, :per_device, tokens:]
    f_real, f_imag = u[:, per_device:, :tokens], u[:, per_device:, tokens:]
    p_real = u_real * f_real - u_imag * f_imag
    p_imag = u_real * f_imag + u_imag * f_real
    product = jnp.concatenate([p_real, p_imag], -1).reshape(outer * per_device, 2 * tokens)
    q = dot(product, backward).reshape(outer, per_device, 2 * tokens)
    q_real, q_imag = q[..., :tokens], q[..., tokens:]
    r_real = q_real * twist_cos - q_imag * twist_sin
    r_imag = q_real * twist_sin + q_imag * twist_cos
    stacked = jnp.stack([r_real, r_imag], 0).reshape(2 * outer, per_device * tokens)
    result = dot(last_table, stacked)
    return result.reshape(blocks, per_device, tokens).astype(jnp.bfloat16)


def causal_short(rows, tail, taps):
    extended = jnp.concatenate([tail, rows], 0)
    return (
        taps[0] * extended[2:].astype(jnp.float32)
        + taps[1] * extended[1:-1].astype(jnp.float32)
        + taps[2] * extended[:-2].astype(jnp.float32)
    )


def body(query_rows, key_rows, value_rows, short_filter, long_filter, skip_gain, out_weight):
    tokens_here, channels = query_rows.shape
    groups = lax.axis_size("seq")
    per_device = channels // groups
    tables = make_tables(groups, tokens_here)
    tails = shifted((query_rows[-2:], key_rows[-2:], value_rows[-2:]), "seq", 1)
    query_mix = causal_short(query_rows, tails[0], short_filter[:, 0, :])
    key_mix = causal_short(key_rows, tails[1], short_filter[:, 1, :])
    value_mix = causal_short(value_rows, tails[2], short_filter[:, 2, :])
    gated = (key_mix * value_mix).astype(jnp.bfloat16)
    gated_cols = gated.T.reshape(groups, per_device, tokens_here)
    filter_cols = long_filter.T.reshape(groups, per_device, tokens_here)
    outgoing = jnp.concatenate([gated_cols, filter_cols], 1)
    pieces = lax.all_to_all(outgoing, "seq", split_axis=0, concat_axis=0, tiled=True)
    mixed = long_conv(pieces, per_device, tables)
    returned = lax.all_to_all(mixed, "seq", split_axis=0, concat_axis=0, tiled=True)
    conv = returned.reshape(channels, tokens_here).T
    inner = (query_mix * (conv.astype(jnp.float32) + skip_gain * gated.astype(jnp.float32))).astype(
        jnp.bfloat16
    )
    weights = lax.all_gather(out_weight, "seq", axis=0, tiled=True)
    total = jnp.dot(
        lax.all_gather(inner, "tp", axis=1, tiled=True), weights, preferred_element_type=jnp.float32
    )
    return total.astype(jnp.bfloat16)


def solution(mesh):
    placed = (
        P("seq", "tp"),
        P("seq", "tp"),
        P("seq", "tp"),
        P(None, None, "tp"),
        P("seq", "tp"),
        P("tp"),
        P("seq", "tp"),
    )
    return jax.shard_map(
        body, mesh=mesh, in_specs=placed, out_specs=P("seq", "tp"), check_vma=False
    )
```

```python
import numpy as np
import jax
import jax.numpy as jnp
from jax import lax
from jax.sharding import PartitionSpec as P

TRANSFORM_PRECISION = lax.Precision.HIGH


def shifted(value, axis, by):
    size = lax.axis_size(axis)
    pairs = [(i, i + by) for i in range(size) if 0 <= i + by < size]
    return lax.ppermute(value, axis, pairs)


def make_tables(blocks, tokens):
    outer = 2 * blocks
    period = outer * tokens
    k1 = np.arange(outer, dtype=np.int64)
    n1 = np.arange(blocks, dtype=np.int64)
    n2 = np.arange(tokens, dtype=np.int64)
    first = 2.0 * np.pi * ((k1[:, None] * n1[None, :]) % outer) / outer
    first_table = np.concatenate([np.cos(first), -np.sin(first)], 0)
    twist = 2.0 * np.pi * ((k1[:, None] * n2[None, :]) % period) / period
    twist_cos = np.cos(twist)[:, None, :]
    twist_sin = np.sin(twist)[:, None, :]
    inner = 2.0 * np.pi * ((n2[:, None] * n2[None, :]) % tokens) / tokens
    b_cos = np.cos(inner)
    b_sin = np.sin(inner)
    forward = np.block([[b_cos, -b_sin], [b_sin, b_cos]])
    backward = np.block([[b_cos, b_sin], [-b_sin, b_cos]])
    last = 2.0 * np.pi * ((n1[:, None] * k1[None, :]) % outer) / outer
    last_table = np.concatenate([np.cos(last), -np.sin(last)], 1) / period
    as32 = lambda a: jnp.asarray(a, jnp.float32)
    return tuple(as32(a) for a in (first_table, twist_cos, twist_sin, forward, backward, last_table))


def dot(a, b):
    return jnp.dot(a, b, precision=TRANSFORM_PRECISION, preferred_element_type=jnp.float32)


def long_conv(pieces, per_device, tables):
    first_table, twist_cos, twist_sin, forward, backward, last_table = tables
    blocks, both, tokens = pieces.shape
    outer = 2 * blocks
    spec = dot(first_table, pieces.reshape(blocks, both * tokens)).reshape(2, outer, both, tokens)
    s_real, s_imag = spec[0], spec[1]
    w_real = s_real * twist_cos + s_imag * twist_sin
    w_imag = s_imag * twist_cos - s_real * twist_sin
    twisted = jnp.concatenate([w_real, w_imag], -1).reshape(outer * both, 2 * tokens)
    u = dot(twisted, forward).reshape(outer, both, 2 * tokens)
    u_real, u_imag = u[:, :per_device, :tokens], u[:, :per_device, tokens:]
    f_real, f_imag = u[:, per_device:, :tokens], u[:, per_device:, tokens:]
    p_real = u_real * f_real - u_imag * f_imag
    p_imag = u_real * f_imag + u_imag * f_real
    product = jnp.concatenate([p_real, p_imag], -1).reshape(outer * per_device, 2 * tokens)
    q = dot(product, backward).reshape(outer, per_device, 2 * tokens)
    q_real, q_imag = q[..., :tokens], q[..., tokens:]
    r_real = q_real * twist_cos - q_imag * twist_sin
    r_imag = q_real * twist_sin + q_imag * twist_cos
    stacked = jnp.stack([r_real, r_imag], 0).reshape(2 * outer, per_device * tokens)
    result = dot(last_table, stacked)
    return result.reshape(blocks, per_device, tokens).astype(jnp.bfloat16)


def causal_short(rows, tail, taps):
    extended = jnp.concatenate([tail, rows], 0)
    return (
        taps[0] * extended[2:].astype(jnp.float32)
        + taps[1] * extended[1:-1].astype(jnp.float32)
        + taps[2] * extended[:-2].astype(jnp.float32)
    )


def block(query_rows, key_rows, value_rows, short_filter, long_filter, skip_gain, out_weight):
    tokens_here, channels = query_rows.shape
    groups = lax.axis_size("seq")
    per_device = channels // groups
    tables = make_tables(groups, tokens_here)
    weights = lax.all_gather(out_weight, "seq", axis=0, tiled=True)
    tails = shifted((query_rows[-2:], key_rows[-2:], value_rows[-2:]), "seq", 1)
    query_mix = causal_short(query_rows, tails[0], short_filter[:, 0, :])
    key_mix = causal_short(key_rows, tails[1], short_filter[:, 1, :])
    value_mix = causal_short(value_rows, tails[2], short_filter[:, 2, :])
    gated = (key_mix * value_mix).astype(jnp.bfloat16)
    gated_cols = gated.T.reshape(groups, per_device, tokens_here)
    filter_cols = long_filter.T.reshape(groups, per_device, tokens_here)
    outgoing = jnp.concatenate([gated_cols, filter_cols], 1)
    pieces = lax.all_to_all(outgoing, "seq", split_axis=0, concat_axis=0, tiled=True)
    mixed = long_conv(pieces, per_device, tables)
    returned = lax.all_to_all(mixed, "seq", split_axis=0, concat_axis=0, tiled=True)
    conv = returned.reshape(channels, tokens_here).T
    inner = (query_mix * (conv.astype(jnp.float32) + skip_gain * gated.astype(jnp.float32))).astype(
        jnp.bfloat16
    )
    total = jnp.dot(
        lax.all_gather(inner, "tp", axis=1, tiled=True), weights, preferred_element_type=jnp.float32
    )
    return total.astype(jnp.bfloat16)


def solution(mesh):
    placed = (
        P("seq", "tp"),
        P("seq", "tp"),
        P("seq", "tp"),
        P(None, None, "tp"),
        P("seq", "tp"),
        P("tp"),
        P("seq", "tp"),
    )
    return jax.shard_map(
        block, mesh=mesh, in_specs=placed, out_specs=P("seq", "tp"), check_vma=False
    )
```

```python
import numpy as np
import jax
import jax.numpy as jnp
from jax import lax
from jax.sharding import PartitionSpec as P

TRANSFORM_PRECISION = lax.Precision.HIGH


def shifted(value, axis, by):
    size = lax.axis_size(axis)
    pairs = [(i, i + by) for i in range(size) if 0 <= i + by < size]
    return lax.ppermute(value, axis, pairs)


def make_tables(blocks, tokens):
    outer = 2 * blocks
    period = outer * tokens
    k1 = np.arange(outer, dtype=np.int64)
    n1 = np.arange(blocks, dtype=np.int64)
    n2 = np.arange(tokens, dtype=np.int64)
    first = 2.0 * np.pi * ((k1[:, None] * n1[None, :]) % outer) / outer
    first_table = np.concatenate([np.cos(first), -np.sin(first)], 0)
    twist = 2.0 * np.pi * ((k1[:, None] * n2[None, :]) % period) / period
    twist_cos = np.cos(twist)[:, None, :]
    twist_sin = np.sin(twist)[:, None, :]
    inner = 2.0 * np.pi * ((n2[:, None] * n2[None, :]) % tokens) / tokens
    b_cos = np.cos(inner)
    b_sin = np.sin(inner)
    forward = np.block([[b_cos, -b_sin], [b_sin, b_cos]])
    backward = np.block([[b_cos, b_sin], [-b_sin, b_cos]])
    last = 2.0 * np.pi * ((n1[:, None] * k1[None, :]) % outer) / outer
    last_table = np.concatenate([np.cos(last), -np.sin(last)], 1) / period
    as32 = lambda a: jnp.asarray(a, jnp.float32)
    return tuple(as32(a) for a in (first_table, twist_cos, twist_sin, forward, backward, last_table))


def dot(a, b):
    return jnp.dot(a, b, precision=TRANSFORM_PRECISION, preferred_element_type=jnp.float32)


def long_conv(pieces, per_device, tables):
    first_table, twist_cos, twist_sin, forward, backward, last_table = tables
    blocks, both, tokens = pieces.shape
    outer = 2 * blocks
    spec = dot(first_table, pieces.reshape(blocks, both * tokens)).reshape(2, outer, both, tokens)
    s_real, s_imag = spec[0], spec[1]
    w_real = s_real * twist_cos + s_imag * twist_sin
    w_imag = s_imag * twist_cos - s_real * twist_sin
    twisted = jnp.concatenate([w_real, w_imag], -1).reshape(outer * both, 2 * tokens)
    u = dot(twisted, forward).reshape(outer, both, 2 * tokens)
    u_real, u_imag = u[:, :per_device, :tokens], u[:, :per_device, tokens:]
    f_real, f_imag = u[:, per_device:, :tokens], u[:, per_device:, tokens:]
    p_real = u_real * f_real - u_imag * f_imag
    p_imag = u_real * f_imag + u_imag * f_real
    product = jnp.concatenate([p_real, p_imag], -1).reshape(outer * per_device, 2 * tokens)
    q = dot(product, backward).reshape(outer, per_device, 2 * tokens)
    q_real, q_imag = q[..., :tokens], q[..., tokens:]
    r_real = q_real * twist_cos - q_imag * twist_sin
    r_imag = q_real * twist_sin + q_imag * twist_cos
    stacked = jnp.stack([r_real, r_imag], 0).reshape(2 * outer, per_device * tokens)
    result = dot(last_table, stacked)
    return result.reshape(blocks, per_device, tokens).astype(jnp.bfloat16)


def causal_short(rows, tail, taps):
    extended = jnp.concatenate([tail, rows], 0)
    return (
        taps[0] * extended[2:].astype(jnp.float32)
        + taps[1] * extended[1:-1].astype(jnp.float32)
        + taps[2] * extended[:-2].astype(jnp.float32)
    )


def mixing(query_rows, key_rows, value_rows, short_filter, long_filter, skip_gain):
    tokens_here, channels = query_rows.shape
    groups = lax.axis_size("seq")
    per_device = channels // groups
    tables = make_tables(groups, tokens_here)
    tails = shifted((query_rows[-2:], key_rows[-2:], value_rows[-2:]), "seq", 1)
    query_mix = causal_short(query_rows, tails[0], short_filter[:, 0, :])
    key_mix = causal_short(key_rows, tails[1], short_filter[:, 1, :])
    value_mix = causal_short(value_rows, tails[2], short_filter[:, 2, :])
    gated = (key_mix * value_mix).astype(jnp.bfloat16)
    gated_cols = gated.T.reshape(groups, per_device, tokens_here)
    filter_cols = long_filter.T.reshape(groups, per_device, tokens_here)
    outgoing = jnp.concatenate([gated_cols, filter_cols], 1)
    pieces = lax.all_to_all(outgoing, "seq", split_axis=0, concat_axis=0, tiled=True)
    mixed = long_conv(pieces, per_device, tables)
    returned = lax.all_to_all(mixed, "seq", split_axis=0, concat_axis=0, tiled=True)
    conv = returned.reshape(channels, tokens_here).T
    return (query_mix * (conv.astype(jnp.float32) + skip_gain * gated.astype(jnp.float32))).astype(
        jnp.bfloat16
    )


def projection(inner, out_weight):
    halves = lax.all_to_all(out_weight, "core", split_axis=1, concat_axis=0, tiled=True)
    weights = lax.all_gather(halves, "sq", axis=0, tiled=True)
    rows = lax.all_gather(inner, "tp", axis=1, tiled=True)
    rows = lax.all_gather(rows, "core", axis=0, tiled=True)
    total = jnp.dot(rows, weights, preferred_element_type=jnp.float32).astype(jnp.bfloat16)
    return lax.all_to_all(total, "core", split_axis=0, concat_axis=1, tiled=True)


def solution(mesh):
    placed = (
        P("seq", "tp"),
        P("seq", "tp"),
        P("seq", "tp"),
        P(None, None, "tp"),
        P("seq", "tp"),
        P("tp"),
        P("seq", "tp"),
    )
    first = jax.shard_map(
        mixing, mesh=mesh, in_specs=placed[:6], out_specs=P("seq", "tp"), check_vma=False
    )
    seq, tp = mesh.axis_names
    cores = 2 if mesh.shape[seq] % 2 == 0 else 1
    paired = jax.sharding.Mesh(
        mesh.devices.reshape(mesh.shape[seq] // cores, cores, mesh.shape[tp]), ("sq", "core", "tp")
    )
    pair_spec = P(("sq", "core"), "tp")
    second = jax.shard_map(
        projection,
        mesh=paired,
        in_specs=(pair_spec, pair_spec),
        out_specs=pair_spec,
        check_vma=False,
    )

    def step(*args):
        return second(first(*args[:6]), args[6])

    return step
```

```python
import numpy as np
import jax
import jax.numpy as jnp
from jax import lax
from jax.sharding import PartitionSpec as P

TRANSFORM_PRECISION = lax.Precision.HIGH


def shifted(value, axis, by):
    size = lax.axis_size(axis)
    pairs = [(i, i + by) for i in range(size) if 0 <= i + by < size]
    return lax.ppermute(value, axis, pairs)


def make_tables(blocks, tokens):
    outer = 2 * blocks
    period = outer * tokens
    k1 = np.arange(outer, dtype=np.int64)
    n1 = np.arange(blocks, dtype=np.int64)
    n2 = np.arange(tokens, dtype=np.int64)
    first = 2.0 * np.pi * ((k1[:, None] * n1[None, :]) % outer) / outer
    first_table = np.concatenate([np.cos(first), -np.sin(first)], 0)
    twist = 2.0 * np.pi * ((k1[:, None] * n2[None, :]) % period) / period
    twist_cos = np.cos(twist)[:, None, :]
    twist_sin = np.sin(twist)[:, None, :]
    inner = 2.0 * np.pi * ((n2[:, None] * n2[None, :]) % tokens) / tokens
    b_cos = np.cos(inner)
    b_sin = np.sin(inner)
    forward = np.block([[b_cos, -b_sin], [b_sin, b_cos]])
    backward = np.block([[b_cos, b_sin], [-b_sin, b_cos]])
    last = 2.0 * np.pi * ((n1[:, None] * k1[None, :]) % outer) / outer
    last_table = np.concatenate([np.cos(last), -np.sin(last)], 1) / period
    as32 = lambda a: jnp.asarray(a, jnp.float32)
    return tuple(as32(a) for a in (first_table, twist_cos, twist_sin, forward, backward, last_table))


def dot(a, b):
    return jnp.dot(a, b, precision=TRANSFORM_PRECISION, preferred_element_type=jnp.float32)


def long_conv(pieces, per_device, tables):
    first_table, twist_cos, twist_sin, forward, backward, last_table = tables
    blocks, both, tokens = pieces.shape
    outer = 2 * blocks
    spec = dot(first_table, pieces.reshape(blocks, both * tokens)).reshape(2, outer, both, tokens)
    s_real, s_imag = spec[0], spec[1]
    w_real = s_real * twist_cos + s_imag * twist_sin
    w_imag = s_imag * twist_cos - s_real * twist_sin
    twisted = jnp.concatenate([w_real, w_imag], -1).reshape(outer * both, 2 * tokens)
    u = dot(twisted, forward).reshape(outer, both, 2 * tokens)
    u_real, u_imag = u[:, :per_device, :tokens], u[:, :per_device, tokens:]
    f_real, f_imag = u[:, per_device:, :tokens], u[:, per_device:, tokens:]
    p_real = u_real * f_real - u_imag * f_imag
    p_imag = u_real * f_imag + u_imag * f_real
    product = jnp.concatenate([p_real, p_imag], -1).reshape(outer * per_device, 2 * tokens)
    q = dot(product, backward).reshape(outer, per_device, 2 * tokens)
    q_real, q_imag = q[..., :tokens], q[..., tokens:]
    r_real = q_real * twist_cos - q_imag * twist_sin
    r_imag = q_real * twist_sin + q_imag * twist_cos
    stacked = jnp.stack([r_real, r_imag], 0).reshape(2 * outer, per_device * tokens)
    result = dot(last_table, stacked)
    return result.reshape(blocks, per_device, tokens).astype(jnp.bfloat16)


def causal_short(rows, tail, taps):
    extended = jnp.concatenate([tail, rows], 0)
    return (
        taps[0] * extended[2:].astype(jnp.float32)
        + taps[1] * extended[1:-1].astype(jnp.float32)
        + taps[2] * extended[:-2].astype(jnp.float32)
    )


def block(query_rows, key_rows, value_rows, short_filter, long_filter, skip_gain, out_weight):
    tokens_here, channels = query_rows.shape
    groups = lax.axis_size("seq")
    per_device = channels // groups
    tables = make_tables(groups, tokens_here)
    weights = lax.all_gather(out_weight, "seq", axis=0, tiled=True)
    tails = shifted((query_rows[-2:], key_rows[-2:], value_rows[-2:]), "seq", 1)
    query_mix = causal_short(query_rows, tails[0], short_filter[:, 0, :])
    key_mix = causal_short(key_rows, tails[1], short_filter[:, 1, :])
    value_mix = causal_short(value_rows, tails[2], short_filter[:, 2, :])
    gated = (key_mix * value_mix).astype(jnp.bfloat16)
    gated_cols = gated.T.reshape(groups, per_device, tokens_here)
    filter_cols = long_filter.T.reshape(groups, per_device, tokens_here)
    outgoing = jnp.concatenate([gated_cols, filter_cols], 1)
    pieces = lax.all_to_all(outgoing, "seq", split_axis=0, concat_axis=0, tiled=True)
    mixed = long_conv(pieces, per_device, tables)
    returned = lax.all_to_all(mixed, "seq", split_axis=0, concat_axis=0, tiled=True)
    conv = returned.reshape(channels, tokens_here).T
    inner = (query_mix * (conv.astype(jnp.float32) + skip_gain * gated.astype(jnp.float32))).astype(
        jnp.bfloat16
    )
    return projection(inner, weights).astype(jnp.bfloat16)


def projection(inner, weights):
    size = lax.axis_size("tp")
    here = lax.axis_index("tp")
    width = inner.shape[1]

    def rows_of(source):
        return lax.dynamic_slice_in_dim(weights, source * width, width, 0)

    arrived = [
        lax.ppermute(inner, "tp", [(j, (j + k) % size) for j in range(size)]) for k in range(1, size)
    ]
    total = jnp.dot(inner, rows_of(here), preferred_element_type=jnp.float32)
    for k, chunk in enumerate(arrived, 1):
        total = total + jnp.dot(chunk, rows_of((here - k) % size), preferred_element_type=jnp.float32)
    return total


def solution(mesh):
    placed = (
        P("seq", "tp"),
        P("seq", "tp"),
        P("seq", "tp"),
        P(None, None, "tp"),
        P("seq", "tp"),
        P("tp"),
        P("seq", "tp"),
    )
    return jax.shard_map(block, mesh=mesh, in_specs=placed, out_specs=P("seq", "tp"), check_vma=False)
```

```python
import numpy as np
import jax
import jax.numpy as jnp
from jax import lax
from jax.sharding import PartitionSpec as P

TRANSFORM_PRECISION = lax.Precision.DEFAULT


def shifted(value, axis, by):
    size = lax.axis_size(axis)
    pairs = [(i, i + by) for i in range(size) if 0 <= i + by < size]
    return lax.ppermute(value, axis, pairs)


def make_tables(blocks, tokens):
    outer = 2 * blocks
    period = outer * tokens
    k1 = np.arange(outer, dtype=np.int64)
    n1 = np.arange(blocks, dtype=np.int64)
    n2 = np.arange(tokens, dtype=np.int64)
    first = 2.0 * np.pi * ((k1[:, None] * n1[None, :]) % outer) / outer
    first_table = np.concatenate([np.cos(first), -np.sin(first)], 0)
    twist = 2.0 * np.pi * ((k1[:, None] * n2[None, :]) % period) / period
    twist_cos = np.cos(twist)[:, None, :]
    twist_sin = np.sin(twist)[:, None, :]
    inner = 2.0 * np.pi * ((n2[:, None] * n2[None, :]) % tokens) / tokens
    b_cos = np.cos(inner)
    b_sin = np.sin(inner)
    forward = np.block([[b_cos, -b_sin], [b_sin, b_cos]])
    backward = np.block([[b_cos, b_sin], [-b_sin, b_cos]])
    last = 2.0 * np.pi * ((n1[:, None] * k1[None, :]) % outer) / outer
    last_cos = np.cos(last) / period
    last_sin = -np.sin(last) / period
    as32 = lambda a: jnp.asarray(a, jnp.float32)
    tables = (first_table, twist_cos, twist_sin, forward, backward, last_cos, last_sin)
    return tuple(as32(a) for a in tables)


def dot(a, b):
    return jnp.dot(a, b, precision=TRANSFORM_PRECISION, preferred_element_type=jnp.float32)


def long_conv(pieces, per_device, tables):
    first_table, twist_cos, twist_sin, forward, backward, last_cos, last_sin = tables
    blocks, both, tokens = pieces.shape
    outer = 2 * blocks
    spec = dot(first_table, pieces.reshape(blocks, both * tokens)).reshape(2, outer, both, tokens)
    s_real, s_imag = spec[0], spec[1]
    w_real = s_real * twist_cos + s_imag * twist_sin
    w_imag = s_imag * twist_cos - s_real * twist_sin
    twisted = jnp.concatenate([w_real, w_imag], -1).reshape(outer * both, 2 * tokens)
    u = dot(twisted, forward).reshape(outer, both, 2 * tokens)
    u_real, u_imag = u[:, :per_device, :tokens], u[:, :per_device, tokens:]
    f_real, f_imag = u[:, per_device:, :tokens], u[:, per_device:, tokens:]
    p_real = u_real * f_real - u_imag * f_imag
    p_imag = u_real * f_imag + u_imag * f_real
    product = jnp.concatenate([p_real, p_imag], -1).reshape(outer * per_device, 2 * tokens)
    q = dot(product, backward).reshape(outer, per_device, 2 * tokens)
    q_real, q_imag = q[..., :tokens], q[..., tokens:]
    r_real = q_real * twist_cos - q_imag * twist_sin
    r_imag = q_real * twist_sin + q_imag * twist_cos
    flat = (outer, per_device * tokens)
    result = dot(last_cos, r_real.reshape(flat)) + dot(last_sin, r_imag.reshape(flat))
    return result.reshape(blocks, per_device, tokens).astype(jnp.bfloat16)


def causal_short(rows, tail, taps):
    extended = jnp.concatenate([tail, rows], 0)
    return (
        taps[0] * extended[2:].astype(jnp.float32)
        + taps[1] * extended[1:-1].astype(jnp.float32)
        + taps[2] * extended[:-2].astype(jnp.float32)
    )


def block(query_rows, key_rows, value_rows, short_filter, long_filter, skip_gain, out_weight):
    tokens_here, channels = query_rows.shape
    groups = lax.axis_size("seq")
    per_device = channels // groups
    tables = make_tables(groups, tokens_here)
    weights = lax.all_gather(out_weight, "seq", axis=0, tiled=True)
    filter_cols = long_filter.T.reshape(groups, per_device, tokens_here)
    filter_piece = lax.all_to_all(filter_cols, "seq", split_axis=0, concat_axis=0, tiled=True)
    tails = shifted((query_rows[-2:], key_rows[-2:], value_rows[-2:]), "seq", 1)
    query_mix = causal_short(query_rows, tails[0], short_filter[:, 0, :])
    key_mix = causal_short(key_rows, tails[1], short_filter[:, 1, :])
    value_mix = causal_short(value_rows, tails[2], short_filter[:, 2, :])
    gated = (key_mix * value_mix).astype(jnp.bfloat16)
    gated_cols = gated.T.reshape(groups, per_device, tokens_here)
    gated_piece = lax.all_to_all(gated_cols, "seq", split_axis=0, concat_axis=0, tiled=True)
    pieces = jnp.concatenate([gated_piece, filter_piece], 1)
    mixed = long_conv(pieces, per_device, tables)
    returned = lax.all_to_all(mixed, "seq", split_axis=0, concat_axis=0, tiled=True)
    conv = returned.reshape(channels, tokens_here).T
    inner = (query_mix * (conv.astype(jnp.float32) + skip_gain * gated.astype(jnp.float32))).astype(
        jnp.bfloat16
    )
    return projection(inner, weights).astype(jnp.bfloat16)


def projection(inner, weights):
    size = lax.axis_size("tp")
    here = lax.axis_index("tp")
    width = inner.shape[1]

    def rows_of(source):
        return lax.dynamic_slice_in_dim(weights, source * width, width, 0)

    arrived = [
        lax.ppermute(inner, "tp", [(j, (j + k) % size) for j in range(size)]) for k in range(1, size)
    ]
    total = jnp.dot(inner, rows_of(here), preferred_element_type=jnp.float32)
    for k, chunk in enumerate(arrived, 1):
        total = total + jnp.dot(chunk, rows_of((here - k) % size), preferred_element_type=jnp.float32)
    return total


def solution(mesh):
    placed = (
        P("seq", "tp"),
        P("seq", "tp"),
        P("seq", "tp"),
        P(None, None, "tp"),
        P("seq", "tp"),
        P("tp"),
        P("seq", "tp"),
    )
    return jax.shard_map(
        block, mesh=mesh, in_specs=placed, out_specs=P("seq", "tp"), check_vma=False
    )
```

```python
import numpy as np
import jax
import jax.numpy as jnp
from jax import lax
from jax.sharding import PartitionSpec as P

TRANSFORM_PRECISION = lax.Precision.HIGH


def shifted(value, axis, by):
    size = lax.axis_size(axis)
    pairs = [(i, i + by) for i in range(size) if 0 <= i + by < size]
    return lax.ppermute(value, axis, pairs)


def make_tables(blocks, tokens):
    outer = 2 * blocks
    period = outer * tokens
    k1 = np.arange(outer, dtype=np.int64)
    n1 = np.arange(blocks, dtype=np.int64)
    n2 = np.arange(tokens, dtype=np.int64)
    first = 2.0 * np.pi * ((k1[:, None] * n1[None, :]) % outer) / outer
    first_table = np.concatenate([np.cos(first), -np.sin(first)], 0)
    twist = 2.0 * np.pi * ((k1[:, None] * n2[None, :]) % period) / period
    twist_cos = np.cos(twist)[:, None, :]
    twist_sin = np.sin(twist)[:, None, :]
    inner = 2.0 * np.pi * ((n2[:, None] * n2[None, :]) % tokens) / tokens
    b_cos = np.cos(inner)
    b_sin = np.sin(inner)
    forward = np.block([[b_cos, -b_sin], [b_sin, b_cos]])
    backward = np.block([[b_cos, b_sin], [-b_sin, b_cos]])
    last = 2.0 * np.pi * ((n1[:, None] * k1[None, :]) % outer) / outer
    last_cos = np.cos(last) / period
    last_sin = -np.sin(last) / period
    as32 = lambda a: jnp.asarray(a, jnp.float32)
    tables = (first_table, twist_cos, twist_sin, forward, backward, last_cos, last_sin)
    return tuple(as32(a) for a in tables)


def dot(a, b):
    return jnp.dot(a, b, precision=TRANSFORM_PRECISION, preferred_element_type=jnp.float32)


def long_conv(pieces, per_device, tables):
    first_table, twist_cos, twist_sin, forward, backward, last_cos, last_sin = tables
    blocks, both, tokens = pieces.shape
    outer = 2 * blocks
    spec = dot(first_table, pieces.reshape(blocks, both * tokens)).reshape(2, outer, both, tokens)
    s_real, s_imag = spec[0], spec[1]
    w_real = s_real * twist_cos + s_imag * twist_sin
    w_imag = s_imag * twist_cos - s_real * twist_sin
    twisted = jnp.concatenate([w_real, w_imag], -1).reshape(outer * both, 2 * tokens)
    u = dot(twisted, forward).reshape(outer, both, 2 * tokens)
    u_real, u_imag = u[:, :per_device, :tokens], u[:, :per_device, tokens:]
    f_real, f_imag = u[:, per_device:, :tokens], u[:, per_device:, tokens:]
    p_real = u_real * f_real - u_imag * f_imag
    p_imag = u_real * f_imag + u_imag * f_real
    product = jnp.concatenate([p_real, p_imag], -1).reshape(outer * per_device, 2 * tokens)
    q = dot(product, backward).reshape(outer, per_device, 2 * tokens)
    q_real, q_imag = q[..., :tokens], q[..., tokens:]
    r_real = q_real * twist_cos - q_imag * twist_sin
    r_imag = q_real * twist_sin + q_imag * twist_cos
    flat = (outer, per_device * tokens)
    result = dot(last_cos, r_real.reshape(flat)) + dot(last_sin, r_imag.reshape(flat))
    return result.reshape(blocks, per_device, tokens).astype(jnp.bfloat16)


def causal_short(rows, tail, taps):
    extended = jnp.concatenate([tail, rows], 0)
    return (
        taps[0] * extended[2:].astype(jnp.float32)
        + taps[1] * extended[1:-1].astype(jnp.float32)
        + taps[2] * extended[:-2].astype(jnp.float32)
    )


def block(query_rows, key_rows, value_rows, short_filter, long_filter, skip_gain, out_weight):
    tokens_here, channels = query_rows.shape
    groups = lax.axis_size("seq")
    per_device = channels // groups
    tables = make_tables(groups, tokens_here)
    weights = lax.all_gather(out_weight, "seq", axis=0, tiled=True)
    tails = shifted((query_rows[-2:], key_rows[-2:], value_rows[-2:]), "seq", 1)
    query_mix = causal_short(query_rows, tails[0], short_filter[:, 0, :])
    key_mix = causal_short(key_rows, tails[1], short_filter[:, 1, :])
    value_mix = causal_short(value_rows, tails[2], short_filter[:, 2, :])
    gated = (key_mix * value_mix).astype(jnp.bfloat16)
    gated_cols = gated.T.reshape(groups, per_device, tokens_here)
    filter_cols = long_filter.T.reshape(groups, per_device, tokens_here)
    outgoing = jnp.concatenate([gated_cols, filter_cols], 1)
    pieces = lax.all_to_all(outgoing, "seq", split_axis=0, concat_axis=0, tiled=True)
    mixed = long_conv(pieces, per_device, tables)
    returned = lax.all_to_all(mixed, "seq", split_axis=0, concat_axis=0, tiled=True)
    conv = returned.reshape(channels, tokens_here).T
    inner = (query_mix * (conv.astype(jnp.float32) + skip_gain * gated.astype(jnp.float32))).astype(
        jnp.bfloat16
    )
    return projection(inner, weights).astype(jnp.bfloat16)


def projection(inner, weights):
    size = lax.axis_size("tp")
    here = lax.axis_index("tp")
    width = inner.shape[1]

    def rows_of(source):
        return lax.dynamic_slice_in_dim(weights, source * width, width, 0)

    arrived = [
        lax.ppermute(inner, "tp", [(j, (j + k) % size) for j in range(size)]) for k in range(1, size)
    ]
    total = jnp.dot(inner, rows_of(here), preferred_element_type=jnp.float32)
    for k, chunk in enumerate(arrived, 1):
        total = total + jnp.dot(chunk, rows_of((here - k) % size), preferred_element_type=jnp.float32)
    return total


def solution(mesh):
    placed = (
        P("seq", "tp"),
        P("seq", "tp"),
        P("seq", "tp"),
        P(None, None, "tp"),
        P("seq", "tp"),
        P("tp"),
        P("seq", "tp"),
    )
    return jax.shard_map(
        block, mesh=mesh, in_specs=placed, out_specs=P("seq", "tp"), check_vma=False
    )
```

```python
import math

import numpy as np
import jax
import jax.numpy as jnp
from jax import lax
from jax.sharding import PartitionSpec as P

TRANSFORM_PRECISION = lax.Precision.HIGH


SEQ = ("zh", "x", "y", "core")
SEQ_SIZES = (2, 4, 4, 2)


def seq_all_to_all(value):
    shape = value.shape
    parts = value.reshape(SEQ_SIZES + shape[1:])
    for dim in (3, 2, 1, 0):
        parts = lax.all_to_all(parts, SEQ[dim], split_axis=dim, concat_axis=dim, tiled=True)
    return parts.reshape(shape)


def shifted(value, axis, by):
    size = math.prod(SEQ_SIZES)
    pairs = [(i, i + by) for i in range(size) if 0 <= i + by < size]
    return lax.ppermute(value, axis, pairs)


def make_tables(blocks, tokens):
    outer = 2 * blocks
    period = outer * tokens
    k1 = np.arange(outer, dtype=np.int64)
    n1 = np.arange(blocks, dtype=np.int64)
    n2 = np.arange(tokens, dtype=np.int64)
    first = 2.0 * np.pi * ((k1[:, None] * n1[None, :]) % outer) / outer
    first_table = np.concatenate([np.cos(first), -np.sin(first)], 0)
    twist = 2.0 * np.pi * ((k1[:, None] * n2[None, :]) % period) / period
    twist_cos = np.cos(twist)[:, None, :]
    twist_sin = np.sin(twist)[:, None, :]
    inner = 2.0 * np.pi * ((n2[:, None] * n2[None, :]) % tokens) / tokens
    b_cos = np.cos(inner)
    b_sin = np.sin(inner)
    forward = np.block([[b_cos, -b_sin], [b_sin, b_cos]])
    backward = np.block([[b_cos, b_sin], [-b_sin, b_cos]])
    last = 2.0 * np.pi * ((n1[:, None] * k1[None, :]) % outer) / outer
    last_cos = np.cos(last) / period
    last_sin = -np.sin(last) / period
    as32 = lambda a: jnp.asarray(a, jnp.float32)
    tables = (first_table, twist_cos, twist_sin, forward, backward, last_cos, last_sin)
    return tuple(as32(a) for a in tables)


def dot(a, b):
    return jnp.dot(a, b, precision=TRANSFORM_PRECISION, preferred_element_type=jnp.float32)


def long_conv(pieces, per_device, tables):
    first_table, twist_cos, twist_sin, forward, backward, last_cos, last_sin = tables
    blocks, both, tokens = pieces.shape
    outer = 2 * blocks
    spec = dot(first_table, pieces.reshape(blocks, both * tokens)).reshape(2, outer, both, tokens)
    s_real, s_imag = spec[0], spec[1]
    w_real = s_real * twist_cos + s_imag * twist_sin
    w_imag = s_imag * twist_cos - s_real * twist_sin
    twisted = jnp.concatenate([w_real, w_imag], -1).reshape(outer * both, 2 * tokens)
    u = dot(twisted, forward).reshape(outer, both, 2 * tokens)
    u_real, u_imag = u[:, :per_device, :tokens], u[:, :per_device, tokens:]
    f_real, f_imag = u[:, per_device:, :tokens], u[:, per_device:, tokens:]
    p_real = u_real * f_real - u_imag * f_imag
    p_imag = u_real * f_imag + u_imag * f_real
    product = jnp.concatenate([p_real, p_imag], -1).reshape(outer * per_device, 2 * tokens)
    q = dot(product, backward).reshape(outer, per_device, 2 * tokens)
    q_real, q_imag = q[..., :tokens], q[..., tokens:]
    r_real = q_real * twist_cos - q_imag * twist_sin
    r_imag = q_real * twist_sin + q_imag * twist_cos
    flat = (outer, per_device * tokens)
    result = dot(last_cos, r_real.reshape(flat)) + dot(last_sin, r_imag.reshape(flat))
    return result.reshape(blocks, per_device, tokens).astype(jnp.bfloat16)


def causal_short(rows, tail, taps):
    extended = jnp.concatenate([tail, rows], 0)
    return (
        taps[0] * extended[2:].astype(jnp.float32)
        + taps[1] * extended[1:-1].astype(jnp.float32)
        + taps[2] * extended[:-2].astype(jnp.float32)
    )


def block(query_rows, key_rows, value_rows, short_filter, long_filter, skip_gain, out_weight):
    tokens_here, channels = query_rows.shape
    groups = math.prod(SEQ_SIZES)
    per_device = channels // groups
    tables = make_tables(groups, tokens_here)
    weights = lax.all_gather(out_weight, SEQ, axis=0, tiled=True)
    tails = shifted((query_rows[-2:], key_rows[-2:], value_rows[-2:]), SEQ, 1)
    query_mix = causal_short(query_rows, tails[0], short_filter[:, 0, :])
    key_mix = causal_short(key_rows, tails[1], short_filter[:, 1, :])
    value_mix = causal_short(value_rows, tails[2], short_filter[:, 2, :])
    gated = (key_mix * value_mix).astype(jnp.bfloat16)
    gated_cols = gated.T.reshape(groups, per_device, tokens_here)
    filter_cols = long_filter.T.reshape(groups, per_device, tokens_here)
    outgoing = jnp.concatenate([gated_cols, filter_cols], 1)
    pieces = seq_all_to_all(outgoing)
    mixed = long_conv(pieces, per_device, tables)
    returned = seq_all_to_all(mixed)
    conv = returned.reshape(channels, tokens_here).T
    inner = (query_mix * (conv.astype(jnp.float32) + skip_gain * gated.astype(jnp.float32))).astype(
        jnp.bfloat16
    )
    return projection(inner, weights).astype(jnp.bfloat16)


def projection(inner, weights):
    size = lax.axis_size("tp")
    here = lax.axis_index("tp")
    width = inner.shape[1]

    def rows_of(source):
        return lax.dynamic_slice_in_dim(weights, source * width, width, 0)

    arrived = [
        lax.ppermute(inner, "tp", [(j, (j + k) % size) for j in range(size)]) for k in range(1, size)
    ]
    total = jnp.dot(inner, rows_of(here), preferred_element_type=jnp.float32)
    for k, chunk in enumerate(arrived, 1):
        total = total + jnp.dot(chunk, rows_of((here - k) % size), preferred_element_type=jnp.float32)
    return total


def solution(mesh):
    _, tp = mesh.axis_names
    split = jax.sharding.Mesh(mesh.devices.reshape(SEQ_SIZES + (mesh.shape[tp],)), SEQ + ("tp",))
    rows = P(SEQ, "tp")
    placed = (rows, rows, rows, P(None, None, "tp"), rows, P("tp"), rows)
    return jax.shard_map(block, mesh=split, in_specs=placed, out_specs=rows, check_vma=False)
```

```python
import numpy as np
import jax
import jax.numpy as jnp
from jax import lax
from jax.sharding import PartitionSpec as P

TRANSFORM_PRECISION = lax.Precision.HIGH


def shifted(value, axis, by):
    size = lax.axis_size(axis)
    pairs = [(i, i + by) for i in range(size) if 0 <= i + by < size]
    return lax.ppermute(value, axis, pairs)


def make_tables(blocks, tokens):
    outer = 2 * blocks
    period = outer * tokens
    k1 = np.arange(outer, dtype=np.int64)
    n1 = np.arange(blocks, dtype=np.int64)
    n2 = np.arange(tokens, dtype=np.int64)
    first = 2.0 * np.pi * ((k1[:, None] * n1[None, :]) % outer) / outer
    first_table = np.concatenate([np.cos(first), -np.sin(first)], 0)
    twist = 2.0 * np.pi * ((k1[:, None] * n2[None, :]) % period) / period
    twist_cos = np.cos(twist)[:, None, :]
    twist_sin = np.sin(twist)[:, None, :]
    inner = 2.0 * np.pi * ((n2[:, None] * n2[None, :]) % tokens) / tokens
    b_cos = np.cos(inner)
    b_sin = np.sin(inner)
    forward = np.block([[b_cos, -b_sin], [b_sin, b_cos]])
    backward = np.block([[b_cos, b_sin], [-b_sin, b_cos]])
    half = tokens // 2
    backward = [
        np.concatenate([backward[:, h * half : (h + 1) * half], backward[:, tokens + h * half :][:, :half]], 1)
        for h in range(2)
    ]
    last = 2.0 * np.pi * ((n1[:, None] * k1[None, :]) % outer) / outer
    last_cos = np.cos(last) / period
    last_sin = -np.sin(last) / period
    as32 = lambda a: jnp.asarray(a, jnp.float32)
    tables = (first_table, twist_cos, twist_sin, forward, *backward, last_cos, last_sin)
    first_table, twist_cos, twist_sin, forward, back_0, back_1, last_cos, last_sin = map(as32, tables)
    return first_table, twist_cos, twist_sin, forward, (back_0, back_1), last_cos, last_sin


def dot(a, b):
    return jnp.dot(a, b, precision=TRANSFORM_PRECISION, preferred_element_type=jnp.float32)


def long_conv(pieces, per_device, tables):
    first_table, twist_cos, twist_sin, forward, backward, last_cos, last_sin = tables
    blocks, both, tokens = pieces.shape
    outer = 2 * blocks
    spec = dot(first_table, pieces.reshape(blocks, both * tokens)).reshape(2, outer, both, tokens)
    s_real, s_imag = spec[0], spec[1]
    w_real = s_real * twist_cos + s_imag * twist_sin
    w_imag = s_imag * twist_cos - s_real * twist_sin
    twisted = jnp.concatenate([w_real, w_imag], -1).reshape(outer * both, 2 * tokens)
    u = dot(twisted, forward).reshape(outer, both, 2 * tokens)
    u_real, u_imag = u[:, :per_device, :tokens], u[:, :per_device, tokens:]
    f_real, f_imag = u[:, per_device:, :tokens], u[:, per_device:, tokens:]
    p_real = u_real * f_real - u_imag * f_imag
    p_imag = u_real * f_imag + u_imag * f_real
    product = jnp.concatenate([p_real, p_imag], -1).reshape(outer * per_device, 2 * tokens)
    half = tokens // 2
    halves = []
    for h, table in enumerate(backward):
        q = dot(product, table).reshape(outer, per_device, 2 * half)
        q_real, q_imag = q[..., :half], q[..., half:]
        t_cos = twist_cos[..., h * half : (h + 1) * half]
        t_sin = twist_sin[..., h * half : (h + 1) * half]
        r_real = q_real * t_cos - q_imag * t_sin
        r_imag = q_real * t_sin + q_imag * t_cos
        flat = (outer, per_device * half)
        result = dot(last_cos, r_real.reshape(flat)) + dot(last_sin, r_imag.reshape(flat))
        halves.append(result.reshape(blocks, per_device, half).astype(jnp.bfloat16))
    return halves


def causal_short(rows, tail, taps):
    extended = jnp.concatenate([tail, rows], 0)
    return (
        taps[0] * extended[2:].astype(jnp.float32)
        + taps[1] * extended[1:-1].astype(jnp.float32)
        + taps[2] * extended[:-2].astype(jnp.float32)
    )


def block(query_rows, key_rows, value_rows, short_filter, long_filter, skip_gain, out_weight):
    tokens_here, channels = query_rows.shape
    groups = lax.axis_size("seq")
    per_device = channels // groups
    tables = make_tables(groups, tokens_here)
    weights = lax.all_gather(out_weight, "seq", axis=0, tiled=True)
    tails = shifted((query_rows[-2:], key_rows[-2:], value_rows[-2:]), "seq", 1)
    query_mix = causal_short(query_rows, tails[0], short_filter[:, 0, :])
    key_mix = causal_short(key_rows, tails[1], short_filter[:, 1, :])
    value_mix = causal_short(value_rows, tails[2], short_filter[:, 2, :])
    gated = (key_mix * value_mix).astype(jnp.bfloat16)
    gated_cols = gated.T.reshape(groups, per_device, tokens_here)
    filter_cols = long_filter.T.reshape(groups, per_device, tokens_here)
    outgoing = jnp.concatenate([gated_cols, filter_cols], 1)
    pieces = lax.all_to_all(outgoing, "seq", split_axis=0, concat_axis=0, tiled=True)
    mixed = long_conv(pieces, per_device, tables)
    half = tokens_here // 2
    outputs = []
    for h, piece in enumerate(mixed):
        back = lax.all_to_all(piece, "seq", split_axis=0, concat_axis=0, tiled=True)
        rows = slice(h * half, (h + 1) * half)
        parts = (back, query_mix[rows], gated[rows], skip_gain)
        back, mix, skip, gain = lax.optimization_barrier(parts)
        conv = back.reshape(channels, half).T.astype(jnp.float32)
        skip = gain * skip.astype(jnp.float32)
        inner = (mix * (conv + skip)).astype(jnp.bfloat16)
        outputs.append(projection(inner, weights).astype(jnp.bfloat16))
    return jnp.concatenate(outputs, 0)


def projection(inner, weights):
    size = lax.axis_size("tp")
    here = lax.axis_index("tp")
    width = inner.shape[1]

    def rows_of(source):
        return lax.dynamic_slice_in_dim(weights, source * width, width, 0)

    arrived = [
        lax.ppermute(inner, "tp", [(j, (j + k) % size) for j in range(size)]) for k in range(1, size)
    ]
    total = jnp.dot(inner, rows_of(here), preferred_element_type=jnp.float32)
    for k, chunk in enumerate(arrived, 1):
        total = total + jnp.dot(chunk, rows_of((here - k) % size), preferred_element_type=jnp.float32)
    return total


def solution(mesh):
    placed = (
        P("seq", "tp"),
        P("seq", "tp"),
        P("seq", "tp"),
        P(None, None, "tp"),
        P("seq", "tp"),
        P("tp"),
        P("seq", "tp"),
    )
    return jax.shard_map(block, mesh=mesh, in_specs=placed, out_specs=P("seq", "tp"), check_vma=False)
```

```python
import numpy as np
import jax
import jax.numpy as jnp
from jax import lax
from jax.sharding import PartitionSpec as P

TRANSFORM_PRECISION = lax.Precision.HIGH


def shifted(value, axis, by):
    size = lax.axis_size(axis)
    pairs = [(i, i + by) for i in range(size) if 0 <= i + by < size]
    return lax.ppermute(value, axis, pairs)


def make_tables(blocks, tokens):
    outer = 2 * blocks
    period = outer * tokens
    k1 = np.arange(outer, dtype=np.int64)
    n1 = np.arange(blocks, dtype=np.int64)
    n2 = np.arange(tokens, dtype=np.int64)
    first = 2.0 * np.pi * ((k1[:, None] * n1[None, :]) % outer) / outer
    first_table = np.concatenate([np.cos(first), -np.sin(first)], 0)
    twist = 2.0 * np.pi * ((k1[:, None] * n2[None, :]) % period) / period
    twist_cos = np.cos(twist)[:, None, :]
    twist_sin = np.sin(twist)[:, None, :]
    inner = 2.0 * np.pi * ((n2[:, None] * n2[None, :]) % tokens) / tokens
    b_cos = np.cos(inner)
    b_sin = np.sin(inner)
    forward = np.block([[b_cos, -b_sin], [b_sin, b_cos]])
    backward = np.block([[b_cos, b_sin], [-b_sin, b_cos]])
    last = 2.0 * np.pi * ((n1[:, None] * k1[None, :]) % outer) / outer
    last_cos = np.cos(last) / period
    last_sin = -np.sin(last) / period
    as32 = lambda a: jnp.asarray(a, jnp.float32)
    twist_cos_t = np.cos(twist).T[None]
    twist_sin_t = np.sin(twist).T[None]
    tables = (
        first_table, twist_cos, twist_sin, forward, backward.T, twist_cos_t, twist_sin_t, last_cos, last_sin
    )
    return tuple(as32(a) for a in tables)


def dot(a, b):
    return jnp.dot(a, b, precision=TRANSFORM_PRECISION, preferred_element_type=jnp.float32)


def einsum(form, a, b):
    return jnp.einsum(form, a, b, precision=TRANSFORM_PRECISION, preferred_element_type=jnp.float32)


def long_conv(pieces, per_device, tables):
    first_table, twist_cos, twist_sin, forward, backward, back_cos, back_sin, last_cos, last_sin = tables
    blocks, both, tokens = pieces.shape
    outer = 2 * blocks
    spec = dot(first_table, pieces.reshape(blocks, both * tokens)).reshape(2, outer, both, tokens)
    s_real, s_imag = spec[0], spec[1]
    w_real = s_real * twist_cos + s_imag * twist_sin
    w_imag = s_imag * twist_cos - s_real * twist_sin
    twisted = jnp.concatenate([w_real, w_imag], -1).reshape(outer * both, 2 * tokens)
    u = dot(twisted, forward).reshape(outer, both, 2 * tokens)
    u_real, u_imag = u[:, :per_device, :tokens], u[:, :per_device, tokens:]
    f_real, f_imag = u[:, per_device:, :tokens], u[:, per_device:, tokens:]
    p_real = u_real * f_real - u_imag * f_imag
    p_imag = u_real * f_imag + u_imag * f_real
    product = jnp.concatenate([p_real, p_imag], -1)
    q = einsum("nq,kcq->cnk", backward, product)
    q_real, q_imag = q[:, :tokens], q[:, tokens:]
    r_real = q_real * back_cos - q_imag * back_sin
    r_imag = q_real * back_sin + q_imag * back_cos
    result = einsum("cnk,mk->cnm", r_real, last_cos) + einsum("cnk,mk->cnm", r_imag, last_sin)
    return result.astype(jnp.bfloat16).transpose(2, 0, 1)


def causal_short(rows, tail, taps):
    extended = jnp.concatenate([tail, rows], 0)
    return (
        taps[0] * extended[2:].astype(jnp.float32)
        + taps[1] * extended[1:-1].astype(jnp.float32)
        + taps[2] * extended[:-2].astype(jnp.float32)
    )


def block(query_rows, key_rows, value_rows, short_filter, long_filter, skip_gain, out_weight):
    tokens_here, channels = query_rows.shape
    groups = lax.axis_size("seq")
    per_device = channels // groups
    tables = make_tables(groups, tokens_here)
    weights = lax.all_gather(out_weight, "seq", axis=0, tiled=True)
    tails = shifted((query_rows[-2:], key_rows[-2:], value_rows[-2:]), "seq", 1)
    query_mix = causal_short(query_rows, tails[0], short_filter[:, 0, :])
    key_mix = causal_short(key_rows, tails[1], short_filter[:, 1, :])
    value_mix = causal_short(value_rows, tails[2], short_filter[:, 2, :])
    gated = (key_mix * value_mix).astype(jnp.bfloat16)
    gated_cols = gated.T.reshape(groups, per_device, tokens_here)
    filter_cols = long_filter.T.reshape(groups, per_device, tokens_here)
    outgoing = jnp.concatenate([gated_cols, filter_cols], 1)
    pieces = lax.all_to_all(outgoing, "seq", split_axis=0, concat_axis=0, tiled=True)
    mixed = long_conv(pieces, per_device, tables)
    returned = lax.all_to_all(mixed, "seq", split_axis=0, concat_axis=0, tiled=True)
    conv = returned.reshape(channels, tokens_here).T
    inner = (query_mix * (conv.astype(jnp.float32) + skip_gain * gated.astype(jnp.float32))).astype(
        jnp.bfloat16
    )
    return projection(inner, weights).astype(jnp.bfloat16)


def projection(inner, weights):
    size = lax.axis_size("tp")
    here = lax.axis_index("tp")
    width = inner.shape[1]

    def rows_of(source):
        return lax.dynamic_slice_in_dim(weights, source * width, width, 0)

    arrived = [
        lax.ppermute(inner, "tp", [(j, (j + k) % size) for j in range(size)]) for k in range(1, size)
    ]
    total = jnp.dot(inner, rows_of(here), preferred_element_type=jnp.float32)
    for k, chunk in enumerate(arrived, 1):
        total = total + jnp.dot(chunk, rows_of((here - k) % size), preferred_element_type=jnp.float32)
    return total


def solution(mesh):
    placed = (
        P("seq", "tp"),
        P("seq", "tp"),
        P("seq", "tp"),
        P(None, None, "tp"),
        P("seq", "tp"),
        P("tp"),
        P("seq", "tp"),
    )
    return jax.shard_map(block, mesh=mesh, in_specs=placed, out_specs=P("seq", "tp"), check_vma=False)
```

```python
import numpy as np
import jax
import jax.numpy as jnp
from jax import lax
from jax.sharding import PartitionSpec as P

TRANSFORM_PRECISION = lax.Precision.HIGH


def shifted(value, axis, by):
    size = lax.axis_size(axis)
    pairs = [(i, i + by) for i in range(size) if 0 <= i + by < size]
    return lax.ppermute(value, axis, pairs)


def make_tables(blocks, tokens):
    outer = 2 * blocks
    period = outer * tokens
    k1 = np.arange(outer, dtype=np.int64)
    n1 = np.arange(blocks, dtype=np.int64)
    n2 = np.arange(tokens, dtype=np.int64)
    first = 2.0 * np.pi * ((k1[:, None] * n1[None, :]) % outer) / outer
    first_table = np.concatenate([np.cos(first), -np.sin(first)], 0)
    twist = 2.0 * np.pi * ((k1[:, None] * n2[None, :]) % period) / period
    twist_cos = np.cos(twist)[:, None, :]
    twist_sin = np.sin(twist)[:, None, :]
    inner = 2.0 * np.pi * ((n2[:, None] * n2[None, :]) % tokens) / tokens
    b_cos = np.cos(inner)
    b_sin = np.sin(inner)
    forward = (b_cos, -b_sin - b_cos, b_cos - b_sin)
    backward = np.block([[b_cos, b_sin], [-b_sin, b_cos]])
    last = 2.0 * np.pi * ((n1[:, None] * k1[None, :]) % outer) / outer
    last_cos = np.cos(last) / period
    last_sin = -np.sin(last) / period
    as32 = lambda a: jnp.asarray(a, jnp.float32)
    twist_cos_t = np.cos(twist).T[None]
    twist_sin_t = np.sin(twist).T[None]
    tables = (
        first_table, twist_cos, twist_sin, forward, backward.T, twist_cos_t, twist_sin_t, last_cos, last_sin
    )
    return tuple(tuple(map(as32, a)) if isinstance(a, tuple) else as32(a) for a in tables)


def dot(a, b):
    return jnp.dot(a, b, precision=TRANSFORM_PRECISION, preferred_element_type=jnp.float32)


def einsum(form, a, b):
    return jnp.einsum(form, a, b, precision=TRANSFORM_PRECISION, preferred_element_type=jnp.float32)


def long_conv(pieces, per_device, tables):
    first_table, twist_cos, twist_sin, forward, backward, back_cos, back_sin, last_cos, last_sin = tables
    blocks, both, tokens = pieces.shape
    outer = 2 * blocks
    spec = dot(first_table, pieces.reshape(blocks, both * tokens)).reshape(2, outer, both, tokens)
    s_real, s_imag = spec[0], spec[1]
    w_real = s_real * twist_cos + s_imag * twist_sin
    w_imag = s_imag * twist_cos - s_real * twist_sin
    flat = (outer * both, tokens)
    w_real, w_imag = w_real.reshape(flat), w_imag.reshape(flat)
    plain, low, high = forward
    first = dot(w_real + w_imag, plain)
    whole_real = (first - dot(w_imag, high)).reshape(outer, both, tokens)
    whole_imag = (first + dot(w_real, low)).reshape(outer, both, tokens)
    u_real, u_imag = whole_real[:, :per_device], whole_imag[:, :per_device]
    f_real, f_imag = whole_real[:, per_device:], whole_imag[:, per_device:]
    p_real = u_real * f_real - u_imag * f_imag
    p_imag = u_real * f_imag + u_imag * f_real
    product = jnp.concatenate([p_real, p_imag], -1)
    q = einsum("nq,kcq->cnk", backward, product)
    q_real, q_imag = q[:, :tokens], q[:, tokens:]
    r_real = q_real * back_cos - q_imag * back_sin
    r_imag = q_real * back_sin + q_imag * back_cos
    result = einsum("cnk,mk->cnm", r_real, last_cos) + einsum("cnk,mk->cnm", r_imag, last_sin)
    return result.astype(jnp.bfloat16).transpose(2, 0, 1)


def causal_short(rows, tail, taps):
    extended = jnp.concatenate([tail, rows], 0)
    return (
        taps[0] * extended[2:].astype(jnp.float32)
        + taps[1] * extended[1:-1].astype(jnp.float32)
        + taps[2] * extended[:-2].astype(jnp.float32)
    )


def block(query_rows, key_rows, value_rows, short_filter, long_filter, skip_gain, out_weight):
    tokens_here, channels = query_rows.shape
    groups = lax.axis_size("seq")
    per_device = channels // groups
    tables = make_tables(groups, tokens_here)
    weights = lax.all_gather(out_weight, "seq", axis=0, tiled=True)
    tails = shifted((query_rows[-2:], key_rows[-2:], value_rows[-2:]), "seq", 1)
    query_mix = causal_short(query_rows, tails[0], short_filter[:, 0, :])
    key_mix = causal_short(key_rows, tails[1], short_filter[:, 1, :])
    value_mix = causal_short(value_rows, tails[2], short_filter[:, 2, :])
    gated = (key_mix * value_mix).astype(jnp.bfloat16)
    gated_cols = gated.T.reshape(groups, per_device, tokens_here)
    filter_cols = long_filter.T.reshape(groups, per_device, tokens_here)
    outgoing = jnp.concatenate([gated_cols, filter_cols], 1)
    pieces = lax.all_to_all(outgoing, "seq", split_axis=0, concat_axis=0, tiled=True)
    mixed = long_conv(pieces, per_device, tables)
    returned = lax.all_to_all(mixed, "seq", split_axis=0, concat_axis=0, tiled=True)
    conv = returned.reshape(channels, tokens_here).T
    inner = (query_mix * (conv.astype(jnp.float32) + skip_gain * gated.astype(jnp.float32))).astype(
        jnp.bfloat16
    )
    return projection(inner, weights).astype(jnp.bfloat16)


def projection(inner, weights):
    size = lax.axis_size("tp")
    here = lax.axis_index("tp")
    width = inner.shape[1]

    def rows_of(source):
        return lax.dynamic_slice_in_dim(weights, source * width, width, 0)

    arrived = [
        lax.ppermute(inner, "tp", [(j, (j + k) % size) for j in range(size)]) for k in range(1, size)
    ]
    total = jnp.dot(inner, rows_of(here), preferred_element_type=jnp.float32)
    for k, chunk in enumerate(arrived, 1):
        total = total + jnp.dot(chunk, rows_of((here - k) % size), preferred_element_type=jnp.float32)
    return total


def solution(mesh):
    placed = (
        P("seq", "tp"),
        P("seq", "tp"),
        P("seq", "tp"),
        P(None, None, "tp"),
        P("seq", "tp"),
        P("tp"),
        P("seq", "tp"),
    )
    return jax.shard_map(block, mesh=mesh, in_specs=placed, out_specs=P("seq", "tp"), check_vma=False)
```

```python
import numpy as np
import jax
import jax.numpy as jnp
from jax import lax
from jax.sharding import PartitionSpec as P

TRANSFORM_PRECISION = lax.Precision.HIGH


def shifted(value, axis, by):
    size = lax.axis_size(axis)
    pairs = [(i, i + by) for i in range(size) if 0 <= i + by < size]
    return lax.ppermute(value, axis, pairs)


def make_tables(blocks, tokens):
    outer = 2 * blocks
    period = outer * tokens
    k1 = np.arange(blocks + 1, dtype=np.int64)
    weight = np.where((k1 == 0) | (k1 == blocks), 1.0, 2.0)
    n1 = np.arange(blocks, dtype=np.int64)
    n2 = np.arange(tokens, dtype=np.int64)
    first = 2.0 * np.pi * ((k1[:, None] * n1[None, :]) % outer) / outer
    first_table = np.concatenate([np.cos(first), -np.sin(first)], 0)
    twist = 2.0 * np.pi * ((k1[:, None] * n2[None, :]) % period) / period
    twist_cos = np.cos(twist)[:, None, :]
    twist_sin = np.sin(twist)[:, None, :]
    inner = 2.0 * np.pi * ((n2[:, None] * n2[None, :]) % tokens) / tokens
    b_cos = np.cos(inner)
    b_sin = np.sin(inner)
    forward = np.block([[b_cos, -b_sin], [b_sin, b_cos]])
    backward = np.block([[b_cos, b_sin], [-b_sin, b_cos]])
    last = 2.0 * np.pi * ((n1[:, None] * k1[None, :]) % outer) / outer
    last_cos = weight * np.cos(last) / period
    last_sin = -weight * np.sin(last) / period
    as32 = lambda a: jnp.asarray(a, jnp.float32)
    twist_cos_t = np.cos(twist).T[None]
    twist_sin_t = np.sin(twist).T[None]
    tables = (
        first_table, twist_cos, twist_sin, forward, backward.T, twist_cos_t, twist_sin_t, last_cos, last_sin
    )
    return tuple(as32(a) for a in tables)


def dot(a, b):
    return jnp.dot(a, b, precision=TRANSFORM_PRECISION, preferred_element_type=jnp.float32)


def einsum(form, a, b):
    return jnp.einsum(form, a, b, precision=TRANSFORM_PRECISION, preferred_element_type=jnp.float32)


def long_conv(pieces, per_device, tables):
    first_table, twist_cos, twist_sin, forward, backward, back_cos, back_sin, last_cos, last_sin = tables
    blocks, both, tokens = pieces.shape
    outer = first_table.shape[0] // 2
    spec = dot(first_table, pieces.reshape(blocks, both * tokens)).reshape(2, outer, both, tokens)
    s_real, s_imag = spec[0], spec[1]
    w_real = s_real * twist_cos + s_imag * twist_sin
    w_imag = s_imag * twist_cos - s_real * twist_sin
    twisted = jnp.concatenate([w_real, w_imag], -1).reshape(outer * both, 2 * tokens)
    u = dot(twisted, forward).reshape(outer, both, 2 * tokens)
    u_real, u_imag = u[:, :per_device, :tokens], u[:, :per_device, tokens:]
    f_real, f_imag = u[:, per_device:, :tokens], u[:, per_device:, tokens:]
    p_real = u_real * f_real - u_imag * f_imag
    p_imag = u_real * f_imag + u_imag * f_real
    product = jnp.concatenate([p_real, p_imag], -1)
    q = einsum("nq,kcq->cnk", backward, product)
    q_real, q_imag = q[:, :tokens], q[:, tokens:]
    r_real = q_real * back_cos - q_imag * back_sin
    r_imag = q_real * back_sin + q_imag * back_cos
    result = einsum("cnk,mk->cnm", r_real, last_cos) + einsum("cnk,mk->cnm", r_imag, last_sin)
    return result.astype(jnp.bfloat16).transpose(2, 0, 1)


def causal_short(rows, tail, taps):
    extended = jnp.concatenate([tail, rows], 0)
    return (
        taps[0] * extended[2:].astype(jnp.float32)
        + taps[1] * extended[1:-1].astype(jnp.float32)
        + taps[2] * extended[:-2].astype(jnp.float32)
    )


def block(query_rows, key_rows, value_rows, short_filter, long_filter, skip_gain, out_weight):
    tokens_here, channels = query_rows.shape
    groups = lax.axis_size("seq")
    per_device = channels // groups
    tables = make_tables(groups, tokens_here)
    weights = lax.all_gather(out_weight, "seq", axis=0, tiled=True)
    ends = jnp.concatenate([query_rows[-2:], key_rows[-2:], value_rows[-2:]], 0)
    tails = jnp.split(shifted(ends, "seq", 1), 3, 0)
    query_mix = causal_short(query_rows, tails[0], short_filter[:, 0, :])
    key_mix = causal_short(key_rows, tails[1], short_filter[:, 1, :])
    value_mix = causal_short(value_rows, tails[2], short_filter[:, 2, :])
    gated = (key_mix * value_mix).astype(jnp.bfloat16)
    gated_cols = gated.T.reshape(groups, per_device, tokens_here)
    filter_cols = long_filter.T.reshape(groups, per_device, tokens_here)
    outgoing = jnp.concatenate([gated_cols, filter_cols], 1)
    pieces = lax.all_to_all(outgoing, "seq", split_axis=0, concat_axis=0, tiled=True)
    mixed = long_conv(pieces, per_device, tables)
    returned = lax.all_to_all(mixed, "seq", split_axis=0, concat_axis=0, tiled=True)
    conv = returned.reshape(channels, tokens_here).T
    inner = (query_mix * (conv.astype(jnp.float32) + skip_gain * gated.astype(jnp.float32))).astype(
        jnp.bfloat16
    )
    return projection(inner, weights).astype(jnp.bfloat16)


def projection(inner, weights):
    size = lax.axis_size("tp")
    here = lax.axis_index("tp")
    width = inner.shape[1]

    def rows_of(source):
        return lax.dynamic_slice_in_dim(weights, source * width, width, 0)

    arrived = [
        lax.ppermute(inner, "tp", [(j, (j + k) % size) for j in range(size)]) for k in range(1, size)
    ]
    total = jnp.dot(inner, rows_of(here), preferred_element_type=jnp.float32)
    for k, chunk in enumerate(arrived, 1):
        total = total + jnp.dot(chunk, rows_of((here - k) % size), preferred_element_type=jnp.float32)
    return total


def solution(mesh):
    placed = (
        P("seq", "tp"),
        P("seq", "tp"),
        P("seq", "tp"),
        P(None, None, "tp"),
        P("seq", "tp"),
        P("tp"),
        P("seq", "tp"),
    )
    return jax.shard_map(block, mesh=mesh, in_specs=placed, out_specs=P("seq", "tp"), check_vma=False)
```

```python
import numpy as np
import jax
import jax.numpy as jnp
from jax import lax
from jax.sharding import PartitionSpec as P

TRANSFORM_PRECISION = lax.Precision.HIGH


def shifted(value, axis, by):
    size = lax.axis_size(axis)
    pairs = [(i, i + by) for i in range(size) if 0 <= i + by < size]
    return lax.ppermute(value, axis, pairs)


def make_tables(blocks, tokens):
    outer = 2 * blocks
    period = outer * tokens
    k1 = np.arange(blocks + 1, dtype=np.int64)
    weight = np.where((k1 == 0) | (k1 == blocks), 1.0, 2.0)
    n1 = np.arange(blocks, dtype=np.int64)
    n2 = np.arange(tokens, dtype=np.int64)
    first = 2.0 * np.pi * ((k1[:, None] * n1[None, :]) % outer) / outer
    first_table = np.concatenate([np.cos(first), -np.sin(first)], 0)
    twist = 2.0 * np.pi * ((k1[:, None] * n2[None, :]) % period) / period
    twist_cos = np.cos(twist)[:, None, :]
    twist_sin = np.sin(twist)[:, None, :]
    inner = 2.0 * np.pi * ((n2[:, None] * n2[None, :]) % tokens) / tokens
    b_cos = np.cos(inner)
    b_sin = np.sin(inner)
    forward = np.block([[b_cos, -b_sin], [b_sin, b_cos]])
    backward = np.block([[b_cos, b_sin], [-b_sin, b_cos]])
    last = 2.0 * np.pi * ((n1[:, None] * k1[None, :]) % outer) / outer
    last_cos = weight * np.cos(last) / period
    last_sin = -weight * np.sin(last) / period
    as32 = lambda a: jnp.asarray(a, jnp.float32)
    twist_cos_t = np.cos(twist).T[None]
    twist_sin_t = np.sin(twist).T[None]
    tables = (
        first_table, twist_cos, twist_sin, forward, backward.T, twist_cos_t, twist_sin_t, last_cos, last_sin
    )
    first_table, *rest = map(as32, tables)
    first_high = first_table.astype(jnp.bfloat16)
    first_low = (first_table - first_high.astype(jnp.float32)).astype(jnp.bfloat16)
    return ((first_high, first_low), *rest)


def dot(a, b):
    return jnp.dot(a, b, precision=TRANSFORM_PRECISION, preferred_element_type=jnp.float32)


def einsum(form, a, b):
    return jnp.einsum(form, a, b, precision=TRANSFORM_PRECISION, preferred_element_type=jnp.float32)


def long_conv(pieces, per_device, tables):
    first_table, twist_cos, twist_sin, forward, backward, back_cos, back_sin, last_cos, last_sin = tables
    blocks, both, tokens = pieces.shape
    outer = first_table[0].shape[0] // 2
    values = pieces.reshape(blocks, both * tokens)
    spec = sum(jnp.dot(t, values, preferred_element_type=jnp.float32) for t in first_table)
    spec = spec.reshape(2, outer, both, tokens)
    s_real, s_imag = spec[0], spec[1]
    w_real = s_real * twist_cos + s_imag * twist_sin
    w_imag = s_imag * twist_cos - s_real * twist_sin
    twisted = jnp.concatenate([w_real, w_imag], -1).reshape(outer * both, 2 * tokens)
    u = dot(twisted, forward).reshape(outer, both, 2 * tokens)
    u_real, u_imag = u[:, :per_device, :tokens], u[:, :per_device, tokens:]
    f_real, f_imag = u[:, per_device:, :tokens], u[:, per_device:, tokens:]
    p_real = u_real * f_real - u_imag * f_imag
    p_imag = u_real * f_imag + u_imag * f_real
    product = jnp.concatenate([p_real, p_imag], -1)
    q = einsum("nq,kcq->cnk", backward, product)
    q_real, q_imag = q[:, :tokens], q[:, tokens:]
    r_real = q_real * back_cos - q_imag * back_sin
    r_imag = q_real * back_sin + q_imag * back_cos
    result = einsum("cnk,mk->cnm", r_real, last_cos) + einsum("cnk,mk->cnm", r_imag, last_sin)
    return result.astype(jnp.bfloat16).transpose(2, 0, 1)


def causal_short(rows, tail, taps):
    extended = jnp.concatenate([tail, rows], 0)
    return (
        taps[0] * extended[2:].astype(jnp.float32)
        + taps[1] * extended[1:-1].astype(jnp.float32)
        + taps[2] * extended[:-2].astype(jnp.float32)
    )


def block(query_rows, key_rows, value_rows, short_filter, long_filter, skip_gain, out_weight):
    tokens_here, channels = query_rows.shape
    groups = lax.axis_size("seq")
    per_device = channels // groups
    tables = make_tables(groups, tokens_here)
    weights = lax.all_gather(out_weight, "seq", axis=0, tiled=True)
    tails = shifted((query_rows[-2:], key_rows[-2:], value_rows[-2:]), "seq", 1)
    query_mix = causal_short(query_rows, tails[0], short_filter[:, 0, :])
    key_mix = causal_short(key_rows, tails[1], short_filter[:, 1, :])
    value_mix = causal_short(value_rows, tails[2], short_filter[:, 2, :])
    gated = (key_mix * value_mix).astype(jnp.bfloat16)
    gated_cols = gated.T.reshape(groups, per_device, tokens_here)
    filter_cols = long_filter.T.reshape(groups, per_device, tokens_here)
    outgoing = jnp.concatenate([gated_cols, filter_cols], 1)
    pieces = lax.all_to_all(outgoing, "seq", split_axis=0, concat_axis=0, tiled=True)
    mixed = long_conv(pieces, per_device, tables)
    returned = lax.all_to_all(mixed, "seq", split_axis=0, concat_axis=0, tiled=True)
    conv = returned.reshape(channels, tokens_here).T
    inner = (query_mix * (conv.astype(jnp.float32) + skip_gain * gated.astype(jnp.float32))).astype(
        jnp.bfloat16
    )
    return projection(inner, weights).astype(jnp.bfloat16)


def projection(inner, weights):
    size = lax.axis_size("tp")
    here = lax.axis_index("tp")
    width = inner.shape[1]

    def rows_of(source):
        return lax.dynamic_slice_in_dim(weights, source * width, width, 0)

    arrived = [
        lax.ppermute(inner, "tp", [(j, (j + k) % size) for j in range(size)]) for k in range(1, size)
    ]
    total = jnp.dot(inner, rows_of(here), preferred_element_type=jnp.float32)
    for k, chunk in enumerate(arrived, 1):
        total = total + jnp.dot(chunk, rows_of((here - k) % size), preferred_element_type=jnp.float32)
    return total


def solution(mesh):
    placed = (
        P("seq", "tp"),
        P("seq", "tp"),
        P("seq", "tp"),
        P(None, None, "tp"),
        P("seq", "tp"),
        P("tp"),
        P("seq", "tp"),
    )
    return jax.shard_map(block, mesh=mesh, in_specs=placed, out_specs=P("seq", "tp"), check_vma=False)
```
